256 devices in a mesh: wave: 8 (over z_lo, y), tile: 32 (over x, z_hi, core).
Axes of the slice: x: 4, y: 4, z: 8 (z_hi: 4, z_lo: 2; z = z_hi * 2 + z_lo), core: 2. Of those that a mesh axis runs over, the one named last changes fastest.
Arguments:
- coefficients: bfloat16 [512, 256, 4096], P('tile', 'wave'), may hold values from -2.09375 to 2.09375
- profile_basis: bfloat16 [4096, 512], replicated, may hold values from -0.26367188 to 0.26367188
- point_spread: bfloat16 [17, 17], replicated, may hold values from 0.0009994507 to 0.0099487305
- observed: bfloat16 [512, 512, 256], P(None, 'tile', 'wave'), may hold values from -6 to 6
Outputs:
- coef_grad: bfloat16 [512, 256, 4096], P('tile', 'wave')
The draws below stay inside these ranges and needn't reach their ends.
All inputs are finite; a program needn't handle non-finite values.
Results may differ from the reference program's by a relative error of at most 0.0058.
Values may be sent and summed in bfloat16 or wider, within the bound.
No kernel may reach another device: no remote copies, remote signals or barrier semaphores. Data moves between devices by JAX's collectives and lax.ppermute only.
A program may use at most 64 MiB of HBM per device.

```python
import math
import jax
import jax.numpy as jnp
from jax import lax

PROFILES = 4096
WAVES = 512
COLS = 256
PSF = 17
ROWS = 512


def levels(key, extent, split, smallest, high):
    factor_of = 1.0
    for position, parts in split:
        steps = jax.random.uniform(jax.random.fold_in(jax.random.fold_in(key, 6), position), (parts,), jnp.float32, smallest / len(split), high / len(split))
        factor_of = factor_of * jnp.repeat(jnp.exp(steps), extent[position] // parts).reshape((-1,) + (1,) * (len(extent) - 1 - position))
    return factor_of


def gaussian(stream_key, dims, width, reach, split=(), kind=jnp.bfloat16):
    gain = levels(stream_key, dims, split, -0.22, 0.18) if split else 1.0
    array = jax.random.normal(stream_key, dims, jnp.float32) * width * gain
    return jnp.minimum(jnp.maximum(array, -reach), reach).astype(kind)


def setup_inputs(seed: int = 0) -> dict:
    splits = jax.random.split(jax.random.key(seed), 5)
    return {
        "coefficients": gaussian(splits[0], (ROWS, COLS, PROFILES), 0.35, 2.09375, ((0, 32), (1, 8))),
        "profile_basis": gaussian(splits[1], (PROFILES, WAVES), (WAVES ** -0.5), 0.26367188),
        "point_spread": jnp.clip(jnp.exp(jax.random.uniform(splits[2], (PSF, PSF), jnp.float32, math.log(0.0009994507), math.log(0.0099487305))), 0.0009994507, 0.0099487305).astype(jnp.bfloat16),
        "observed": gaussian(splits[3], (WAVES, ROWS, COLS), 1.0, 6.0, ((1, 32), (2, 8))),
    }


def blur_planes(field, kernel):
    half_width = kernel.shape[0] // 2
    result = lax.conv_general_dilated(field[:, None], kernel[None, None], (1, 1), ((half_width, half_width), (half_width, half_width)), precision=lax.Precision.HIGHEST)
    return result[:, 0]


def reference(coefficients, profile_basis, point_spread, observed):
    opacity = jnp.dot(coefficients.reshape(-1, PROFILES), profile_basis, preferred_element_type=jnp.float32)
    spectra = jnp.exp(-opacity).astype(jnp.bfloat16).reshape(ROWS, COLS, WAVES).transpose(2, 0, 1)
    kernel_f = point_spread.astype(jnp.float32)
    blurred = blur_planes(spectra.astype(jnp.float32), kernel_f)
    residual = (blurred - observed.astype(jnp.float32)).astype(jnp.bfloat16)
    adjoint_field = blur_planes(residual.astype(jnp.float32), kernel_f[::-1, ::-1])
    tau_grad = (-spectra.astype(jnp.float32) * adjoint_field).astype(jnp.bfloat16)
    pixel_grad = tau_grad.transpose(1, 2, 0).reshape(-1, WAVES)
    coef_grad = jnp.dot(pixel_grad, profile_basis.T, preferred_element_type=jnp.float32)
    return coef_grad.astype(jnp.bfloat16).reshape(ROWS, COLS, PROFILES)
```

```python
import jax
import jax.numpy as jnp
from jax import lax
from jax.sharding import PartitionSpec as P


def send(block, tile_step, wave_step):
    n_tile = lax.axis_size("tile")
    n_wave = lax.axis_size("wave")
    if wave_step == 0:
        pairs = [(t, t + tile_step) for t in range(n_tile) if 0 <= t + tile_step < n_tile]
        return lax.ppermute(block, "tile", pairs)
    if tile_step == 0:
        pairs = [(w, w + wave_step) for w in range(n_wave) if 0 <= w + wave_step < n_wave]
        return lax.ppermute(block, "wave", pairs)
    pairs = []
    for t in range(n_tile):
        for w in range(n_wave):
            t2, w2 = t + tile_step, w + wave_step
            if 0 <= t2 < n_tile and 0 <= w2 < n_wave:
                pairs.append((w * n_tile + t, w2 * n_tile + t2))
    return lax.ppermute(block, ("wave", "tile"), pairs)


def halo(block, h):
    rows, cols = block.shape[0], block.shape[1]
    low, high = block[rows - h :], block[:h]
    pieces = [
        send(low[:, cols - h :], 1, 1),
        send(low, 1, 0),
        send(low[:, :h], 1, -1),
        send(high[:, cols - h :], -1, 1),
        send(high, -1, 0),
        send(high[:, :h], -1, -1),
        send(block[:, cols - h :], 0, 1),
        send(block[:, :h], 0, -1),
    ]
    return jnp.concatenate([p.reshape(-1, p.shape[-1]) for p in pieces], axis=0)


def blur_mats(psf, rows, cols, h):
    k = psf.shape[0]
    win_rows, win_cols = rows + 2 * h, cols + 2 * h
    shape_c = (k, cols, win_cols)
    col_gap = lax.broadcasted_iota(jnp.int32, shape_c, 2) - lax.broadcasted_iota(jnp.int32, shape_c, 1)
    col_hot = (col_gap == lax.broadcasted_iota(jnp.int32, shape_c, 0)).astype(psf.dtype)
    col = jnp.einsum("ab,bxX->axX", psf, col_hot, preferred_element_type=jnp.float32).astype(psf.dtype)
    shape_r = (k, rows, win_rows)
    row_gap = lax.broadcasted_iota(jnp.int32, shape_r, 2) - lax.broadcasted_iota(jnp.int32, shape_r, 1)
    row_hot = (row_gap == lax.broadcasted_iota(jnp.int32, shape_r, 0)).astype(psf.dtype)
    full = jnp.einsum("ayY,axX->yxYX", row_hot, col, preferred_element_type=jnp.float32)
    full = full.astype(psf.dtype).reshape(rows * cols, win_rows, win_cols)
    center = full[:, h : h + rows, h : h + cols].reshape(rows * cols, rows * cols)
    top, bottom, mid = full[:, :h], full[:, h + rows :], full[:, h : h + rows]
    parts = [
        top[:, :, :h],
        top[:, :, h : h + cols],
        top[:, :, h + cols :],
        bottom[:, :, :h],
        bottom[:, :, h : h + cols],
        bottom[:, :, h + cols :],
        mid[:, :, :h],
        mid[:, :, h + cols :],
    ]
    side = jnp.concatenate([p.reshape(rows * cols, -1) for p in parts], axis=1)
    return center, side


def blur(field, mats, h):
    center, side = mats
    rows, cols, waves = field.shape
    flat = field.reshape(rows * cols, waves)
    near = halo(field, h)
    inner = jnp.dot(center, flat, preferred_element_type=jnp.float32)
    return inner + jnp.dot(side, near, preferred_element_type=jnp.float32)


def shards(coefficients, profile_basis, point_spread, observed):
    rows, cols, profiles = coefficients.shape
    waves = profile_basis.shape[1]
    h = point_spread.shape[0] // 2
    opacity = jnp.dot(
        coefficients.reshape(rows * cols, profiles), profile_basis, preferred_element_type=jnp.float32
    )
    spectra = jnp.exp(-opacity).astype(jnp.bfloat16)
    forward = blur_mats(point_spread, rows, cols, h)
    adjoint = blur_mats(point_spread[::-1, ::-1], rows, cols, h)
    blurred = blur(spectra.reshape(rows, cols, waves), forward, h)
    measured = observed.transpose(1, 2, 0).reshape(rows * cols, waves).astype(jnp.float32)
    residual = (blurred - measured).astype(jnp.bfloat16)
    adjoint_field = blur(residual.reshape(rows, cols, waves), adjoint, h)
    tau_grad = (-spectra.astype(jnp.float32) * adjoint_field).astype(jnp.bfloat16)
    coef_grad = lax.dot_general(
        tau_grad, profile_basis, (((1,), (1,)), ((), ())), preferred_element_type=jnp.float32
    )
    return coef_grad.astype(jnp.bfloat16).reshape(rows, cols, profiles)


def solution(mesh):
    placed = (P("tile", "wave", None), P(), P(), P(None, "tile", "wave"))
    return jax.shard_map(
        shards, mesh=mesh, in_specs=placed, out_specs=P("tile", "wave", None), check_vma=False
    )
```

```python
import jax
import jax.numpy as jnp
from jax import lax
from jax.sharding import PartitionSpec as P


def send(block, axis, step):
    count = lax.axis_size(axis)
    pairs = [(i, i + step) for i in range(count) if 0 <= i + step < count]
    return lax.ppermute(block, axis, pairs)


def window(block, h):
    rows, cols = block.shape[0], block.shape[1]
    left = send(block[:, cols - h :], "wave", 1)
    right = send(block[:, :h], "wave", -1)
    band = jnp.concatenate([left, block, right], axis=1)
    top = send(band[rows - h :], "tile", 1)
    bottom = send(band[:h], "tile", -1)
    full = jnp.concatenate([top, band, bottom], axis=0)
    return full.reshape(-1, full.shape[-1])


def blur_mat(psf, rows, cols, h):
    k = psf.shape[0]
    win_cols = cols + 2 * h
    shape_c = (cols, k, win_cols)
    col_gap = lax.broadcasted_iota(jnp.int32, shape_c, 2) - lax.broadcasted_iota(jnp.int32, shape_c, 0)
    taps = jnp.broadcast_to(psf[None], (cols, k, k))
    strip = jnp.zeros(shape_c, psf.dtype)
    for b in range(k):
        strip = jnp.where(col_gap == b, taps[:, :, b : b + 1], strip)
    strip = strip.reshape(cols, k * win_cols)
    total = (rows + 2 * h) * win_cols
    blocks = [
        jnp.pad(strip, ((0, 0), (y * win_cols, total - y * win_cols - k * win_cols)))
        for y in range(rows)
    ]
    return jnp.concatenate(blocks, axis=0)


def blur(field, mat, h):
    near = window(field, h)
    return jnp.dot(mat, near, preferred_element_type=jnp.float32)


def shards(coefficients, profile_basis, point_spread, observed):
    rows, cols, profiles = coefficients.shape
    waves = profile_basis.shape[1]
    h = point_spread.shape[0] // 2
    opacity = jnp.dot(
        coefficients.reshape(rows * cols, profiles), profile_basis, preferred_element_type=jnp.float32
    )
    spectra = jnp.exp(-opacity).astype(jnp.bfloat16)
    forward = blur_mat(point_spread, rows, cols, h)
    adjoint = blur_mat(point_spread[::-1, ::-1], rows, cols, h)
    blurred = blur(spectra.reshape(rows, cols, waves), forward, h)
    measured = observed.transpose(1, 2, 0).reshape(rows * cols, waves).astype(jnp.float32)
    residual = (blurred - measured).astype(jnp.bfloat16)
    adjoint_field = blur(residual.reshape(rows, cols, waves), adjoint, h)
    tau_grad = (-spectra.astype(jnp.float32) * adjoint_field).astype(jnp.bfloat16)
    coef_grad = lax.dot_general(
        tau_grad, profile_basis, (((1,), (1,)), ((), ())), preferred_element_type=jnp.float32
    )
    return coef_grad.astype(jnp.bfloat16).reshape(rows, cols, profiles)


def solution(mesh):
    placed = (P("tile", "wave", None), P(), P(), P(None, "tile", "wave"))
    return jax.shard_map(
        shards, mesh=mesh, in_specs=placed, out_specs=P("tile", "wave", None), check_vma=False
    )
```

```python
import jax
import jax.numpy as jnp
from jax import lax
from jax.sharding import PartitionSpec as P


def send(block, axis, step):
    count = lax.axis_size(axis)
    pairs = [(i, i + step) for i in range(count) if 0 <= i + step < count]
    return lax.ppermute(block, axis, pairs)


def window(block, h):
    rows, cols = block.shape[0], block.shape[1]
    top = send(block[rows - h :], "tile", 1)
    bottom = send(block[:h], "tile", -1)
    band = jnp.concatenate([top, block, bottom], axis=0)
    left = send(band[:, cols - h :], "wave", 1)
    right = send(band[:, :h], "wave", -1)
    return jnp.concatenate([left, band, right], axis=1)


def blur_mat(psf, group, cols, h):
    k = psf.shape[0]
    win_cols = cols + 2 * h
    shape_c = (cols, k, win_cols)
    col_gap = lax.broadcasted_iota(jnp.int32, shape_c, 2) - lax.broadcasted_iota(jnp.int32, shape_c, 0)
    hot = (col_gap == lax.broadcasted_iota(jnp.int32, shape_c, 1)).astype(psf.dtype)
    strip = jnp.einsum("ab,xbX->xaX", psf, hot, preferred_element_type=jnp.float32)
    strip = strip.astype(psf.dtype).reshape(cols, k * win_cols)
    total = (group + 2 * h) * win_cols
    blocks = [
        jnp.pad(strip, ((0, 0), (y * win_cols, total - y * win_cols - k * win_cols)))
        for y in range(group)
    ]
    return jnp.concatenate(blocks, axis=0)


def blur(field, mat, group, h):
    rows, cols, waves = field.shape
    near = window(field, h)
    win_cols = cols + 2 * h
    flat = near.reshape(-1, waves)
    span = (group + 2 * h) * win_cols
    outs = [
        jnp.dot(mat, flat[g * win_cols : g * win_cols + span], preferred_element_type=jnp.float32)
        for g in range(0, rows, group)
    ]
    return jnp.concatenate(outs, axis=0)


def shards(coefficients, profile_basis, point_spread, observed):
    rows, cols, profiles = coefficients.shape
    waves = profile_basis.shape[1]
    h = point_spread.shape[0] // 2
    opacity = jnp.dot(
        coefficients.reshape(rows * cols, profiles), profile_basis, preferred_element_type=jnp.float32
    )
    spectra = jnp.exp(-opacity).astype(jnp.bfloat16)
    group = 4 if rows % 4 == 0 else rows
    forward = blur_mat(point_spread, group, cols, h)
    adjoint = blur_mat(point_spread[::-1, ::-1], group, cols, h)
    blurred = blur(spectra.reshape(rows, cols, waves), forward, group, h)
    measured = observed.transpose(1, 2, 0).reshape(rows * cols, waves).astype(jnp.float32)
    residual = (blurred - measured).astype(jnp.bfloat16)
    adjoint_field = blur(residual.reshape(rows, cols, waves), adjoint, group, h)
    tau_grad = (-spectra.astype(jnp.float32) * adjoint_field).astype(jnp.bfloat16)
    coef_grad = lax.dot_general(
        tau_grad, profile_basis, (((1,), (1,)), ((), ())), preferred_element_type=jnp.float32
    )
    return coef_grad.astype(jnp.bfloat16).reshape(rows, cols, profiles)


def solution(mesh):
    placed = (P("tile", "wave", None), P(), P(), P(None, "tile", "wave"))
    return jax.shard_map(
        shards, mesh=mesh, in_specs=placed, out_specs=P("tile", "wave", None), check_vma=False
    )
```

```python
import jax
import jax.numpy as jnp
from jax import lax
from jax.sharding import PartitionSpec as P


def send(block, axis, step):
    count = lax.axis_size(axis)
    pairs = [(i, i + step) for i in range(count) if 0 <= i + step < count]
    return lax.ppermute(block, axis, pairs)


def window(block, h):
    rows, cols = block.shape[0], block.shape[1]
    top = send(block[rows - h :], "tile", 1)
    bottom = send(block[:h], "tile", -1)
    band = jnp.concatenate([top, block, bottom], axis=0)
    left = send(band[:, cols - h :], "wave", 1)
    right = send(band[:, :h], "wave", -1)
    return jnp.concatenate([left, band, right], axis=1)


def blur_mat(psf, group, cols, h):
    k = psf.shape[0]
    win_cols = cols + 2 * h
    shape_c = (cols, k, win_cols)
    col_gap = lax.broadcasted_iota(jnp.int32, shape_c, 2) - lax.broadcasted_iota(jnp.int32, shape_c, 0)
    hot = (col_gap == lax.broadcasted_iota(jnp.int32, shape_c, 1)).astype(psf.dtype)
    strip = jnp.einsum("ab,xbX->xaX", psf, hot, preferred_element_type=jnp.float32)
    strip = strip.astype(psf.dtype).reshape(cols, k * win_cols)
    total = (group + 2 * h) * win_cols
    blocks = [
        jnp.pad(strip, ((0, 0), (y * win_cols, total - y * win_cols - k * win_cols)))
        for y in range(group)
    ]
    return jnp.concatenate(blocks, axis=0)


def blur(near, mat, group, out_rows, out_cols, h):
    waves = near.shape[-1]
    win_cols = out_cols + 2 * h
    flat = near.reshape(-1, waves)
    span = (group + 2 * h) * win_cols
    outs = [
        jnp.dot(mat, flat[g * win_cols : g * win_cols + span], preferred_element_type=jnp.float32)
        for g in range(0, out_rows, group)
    ]
    return jnp.concatenate(outs, axis=0)


def inside(rows, cols, h):
    top = lax.axis_index("tile") * rows - h
    left = lax.axis_index("wave") * cols - h
    shape = (rows + 2 * h, cols + 2 * h, 1)
    r = lax.broadcasted_iota(jnp.int32, shape, 0) + top
    c = lax.broadcasted_iota(jnp.int32, shape, 1) + left
    total_r = lax.axis_size("tile") * rows
    total_c = lax.axis_size("wave") * cols
    return (r >= 0) & (r < total_r) & (c >= 0) & (c < total_c)


def shards(coefficients, profile_basis, point_spread, observed):
    rows, cols, profiles = coefficients.shape
    waves = profile_basis.shape[1]
    h = point_spread.shape[0] // 2
    measured = window(observed.transpose(1, 2, 0), h)
    opacity = jnp.dot(
        coefficients.reshape(rows * cols, profiles), profile_basis, preferred_element_type=jnp.float32
    )
    spectra = jnp.exp(-opacity).astype(jnp.bfloat16)
    group = 4 if rows % 4 == 0 else rows
    forward = blur_mat(point_spread, group, cols + 2 * h, h)
    adjoint = blur_mat(point_spread[::-1, ::-1], group, cols, h)
    near = window(spectra.reshape(rows, cols, waves), 2 * h)
    blurred = blur(near, forward, group, rows + 2 * h, cols + 2 * h, h)
    blurred = blurred.reshape(rows + 2 * h, cols + 2 * h, waves)
    residual = (blurred - measured.astype(jnp.float32)).astype(jnp.bfloat16)
    residual = jnp.where(inside(rows, cols, h), residual, jnp.zeros_like(residual))
    adjoint_field = blur(residual, adjoint, group, rows, cols, h)
    tau_grad = (-spectra.astype(jnp.float32) * adjoint_field).astype(jnp.bfloat16)
    coef_grad = lax.dot_general(
        tau_grad, profile_basis, (((1,), (1,)), ((), ())), preferred_element_type=jnp.float32
    )
    return coef_grad.astype(jnp.bfloat16).reshape(rows, cols, profiles)


def solution(mesh):
    placed = (P("tile", "wave", None), P(), P(), P(None, "tile", "wave"))
    return jax.shard_map(
        shards, mesh=mesh, in_specs=placed, out_specs=P("tile", "wave", None), check_vma=False
    )
```

```python
import jax
import jax.numpy as jnp
from jax import lax
from jax.sharding import PartitionSpec as P


def send(block, axis, step):
    count = lax.axis_size(axis)
    pairs = [(i, i + step) for i in range(count) if 0 <= i + step < count]
    return lax.ppermute(block, axis, pairs)


def window(block, h):
    rows, cols = block.shape[0], block.shape[1]
    top = send(block[rows - h :], "tile", 1)
    bottom = send(block[:h], "tile", -1)
    band = jnp.concatenate([top, block, bottom], axis=0)
    left = send(band[:, cols - h :], "wave", 1)
    right = send(band[:, :h], "wave", -1)
    return jnp.concatenate([left, band, right], axis=1)


def blur_mat(psf, group, cols, h):
    k = psf.shape[0]
    win_cols = cols + 2 * h
    shape_c = (cols, k, win_cols)
    col_gap = lax.broadcasted_iota(jnp.int32, shape_c, 2) - lax.broadcasted_iota(jnp.int32, shape_c, 0)
    hot = (col_gap == lax.broadcasted_iota(jnp.int32, shape_c, 1)).astype(psf.dtype)
    strip = jnp.einsum("ab,xbX->xaX", psf, hot, preferred_element_type=jnp.float32)
    strip = strip.astype(psf.dtype).reshape(cols, k * win_cols)
    total = (group + 2 * h) * win_cols
    blocks = [
        jnp.pad(strip, ((0, 0), (y * win_cols, total - y * win_cols - k * win_cols)))
        for y in range(group)
    ]
    return jnp.concatenate(blocks, axis=0)


def blur(near, mat, group, out_rows, out_cols, h):
    waves = near.shape[-1]
    win_cols = out_cols + 2 * h
    flat = near.reshape(-1, waves)
    span = (group + 2 * h) * win_cols
    outs = [
        jnp.dot(mat, flat[g * win_cols : g * win_cols + span], preferred_element_type=jnp.float32)
        for g in range(0, out_rows, group)
    ]
    return jnp.concatenate(outs, axis=0)


def inside(rows, cols, h):
    top = lax.axis_index("tile") * rows - h
    left = lax.axis_index("wave") * cols - h
    shape = (rows + 2 * h, cols + 2 * h, 1)
    r = lax.broadcasted_iota(jnp.int32, shape, 0) + top
    c = lax.broadcasted_iota(jnp.int32, shape, 1) + left
    total_r = lax.axis_size("tile") * rows
    total_c = lax.axis_size("wave") * cols
    return (r >= 0) & (r < total_r) & (c >= 0) & (c < total_c)


def windows(spectra, measured, h):
    rows, cols, waves = spectra.shape
    wide = 2 * h
    down = jnp.concatenate([spectra[rows - wide :], measured[rows - h :]], axis=0)
    up = jnp.concatenate([spectra[:wide], measured[:h]], axis=0)
    above = send(down, "tile", 1)
    below = send(up, "tile", -1)
    band_s = jnp.concatenate([above[:wide], spectra, below[:wide]], axis=0)
    band_m = jnp.concatenate([above[wide:], measured, below[wide:]], axis=0)
    split = band_s.shape[0] * wide

    def edge(lo, hi_s, hi_m):
        return jnp.concatenate(
            [band_s[:, lo : lo + wide].reshape(-1, waves), band_m[:, hi_m : hi_m + h].reshape(-1, waves)],
            axis=0,
        )

    left = send(edge(cols - wide, None, cols - h), "wave", 1)
    right = send(edge(0, None, 0), "wave", -1)

    def parts(piece):
        return (
            piece[:split].reshape(band_s.shape[0], wide, waves),
            piece[split:].reshape(band_m.shape[0], h, waves),
        )

    left_s, left_m = parts(left)
    right_s, right_m = parts(right)
    near_s = jnp.concatenate([left_s, band_s, right_s], axis=1)
    near_m = jnp.concatenate([left_m, band_m, right_m], axis=1)
    return near_s, near_m


def shards(coefficients, profile_basis, point_spread, observed):
    rows, cols, profiles = coefficients.shape
    waves = profile_basis.shape[1]
    h = point_spread.shape[0] // 2
    opacity = jnp.dot(
        coefficients.reshape(rows * cols, profiles), profile_basis, preferred_element_type=jnp.float32
    )
    spectra = jnp.exp(-opacity).astype(jnp.bfloat16)
    group = 4 if rows % 4 == 0 else rows
    forward = blur_mat(point_spread, group, cols + 2 * h, h)
    adjoint = blur_mat(point_spread[::-1, ::-1], group, cols, h)
    near, measured = windows(spectra.reshape(rows, cols, waves), observed.transpose(1, 2, 0), h)
    blurred = blur(near, forward, group, rows + 2 * h, cols + 2 * h, h)
    blurred = blurred.reshape(rows + 2 * h, cols + 2 * h, waves)
    residual = (blurred - measured.astype(jnp.float32)).astype(jnp.bfloat16)
    residual = jnp.where(inside(rows, cols, h), residual, jnp.zeros_like(residual))
    adjoint_field = blur(residual, adjoint, group, rows, cols, h)
    tau_grad = (-spectra.astype(jnp.float32) * adjoint_field).astype(jnp.bfloat16)
    coef_grad = lax.dot_general(
        tau_grad, profile_basis, (((1,), (1,)), ((), ())), preferred_element_type=jnp.float32
    )
    return coef_grad.astype(jnp.bfloat16).reshape(rows, cols, profiles)


def solution(mesh):
    placed = (P("tile", "wave", None), P(), P(), P(None, "tile", "wave"))
    return jax.shard_map(
        shards, mesh=mesh, in_specs=placed, out_specs=P("tile", "wave", None), check_vma=False
    )
```

```python
import jax
import jax.numpy as jnp
from jax import lax
from jax.sharding import PartitionSpec as P


def send(block, axis, step):
    count = lax.axis_size(axis)
    pairs = [(i, i + step) for i in range(count) if 0 <= i + step < count]
    return lax.ppermute(block, axis, pairs)


def window(block, h):
    rows, cols = block.shape[0], block.shape[1]
    top = send(block[rows - h :], "tile", 1)
    bottom = send(block[:h], "tile", -1)
    left = send(block[:, cols - h :], "wave", 1)
    right = send(block[:, :h], "wave", -1)
    corner_left = send(jnp.concatenate([top[:, cols - h :], bottom[:, cols - h :]], axis=0), "wave", 1)
    corner_right = send(jnp.concatenate([top[:, :h], bottom[:, :h]], axis=0), "wave", -1)
    upper = jnp.concatenate([corner_left[:h], top, corner_right[:h]], axis=1)
    middle = jnp.concatenate([left, block, right], axis=1)
    lower = jnp.concatenate([corner_left[h:], bottom, corner_right[h:]], axis=1)
    return jnp.concatenate([upper, middle, lower], axis=0)


def blur_mat(psf, group, cols, h):
    k = psf.shape[0]
    win_cols = cols + 2 * h
    shape_c = (cols, k, win_cols)
    col_gap = lax.broadcasted_iota(jnp.int32, shape_c, 2) - lax.broadcasted_iota(jnp.int32, shape_c, 0)
    hot = (col_gap == lax.broadcasted_iota(jnp.int32, shape_c, 1)).astype(psf.dtype)
    strip = jnp.einsum("ab,xbX->xaX", psf, hot, preferred_element_type=jnp.float32)
    strip = strip.astype(psf.dtype).reshape(cols, k * win_cols)
    total = (group + 2 * h) * win_cols
    blocks = [
        jnp.pad(strip, ((0, 0), (y * win_cols, total - y * win_cols - k * win_cols)))
        for y in range(group)
    ]
    return jnp.concatenate(blocks, axis=0)


def blur(field, mat, group, h):
    rows, cols, waves = field.shape
    near = window(field, h)
    win_cols = cols + 2 * h
    flat = near.reshape(-1, waves)
    span = (group + 2 * h) * win_cols
    outs = [
        jnp.dot(mat, flat[g * win_cols : g * win_cols + span], preferred_element_type=jnp.float32)
        for g in range(0, rows, group)
    ]
    return jnp.concatenate(outs, axis=0)


def shards(coefficients, profile_basis, point_spread, observed):
    rows, cols, profiles = coefficients.shape
    waves = profile_basis.shape[1]
    h = point_spread.shape[0] // 2
    opacity = jnp.dot(
        coefficients.reshape(rows * cols, profiles), profile_basis, preferred_element_type=jnp.float32
    )
    spectra = jnp.exp(-opacity).astype(jnp.bfloat16)
    group = 4 if rows % 4 == 0 else rows
    forward = blur_mat(point_spread, group, cols, h)
    adjoint = blur_mat(point_spread[::-1, ::-1], group, cols, h)
    blurred = blur(spectra.reshape(rows, cols, waves), forward, group, h)
    measured = observed.transpose(1, 2, 0).reshape(rows * cols, waves).astype(jnp.float32)
    residual = (blurred - measured).astype(jnp.bfloat16)
    adjoint_field = blur(residual.reshape(rows, cols, waves), adjoint, group, h)
    tau_grad = (-spectra.astype(jnp.float32) * adjoint_field).astype(jnp.bfloat16)
    coef_grad = lax.dot_general(
        tau_grad, profile_basis, (((1,), (1,)), ((), ())), preferred_element_type=jnp.float32
    )
    return coef_grad.astype(jnp.bfloat16).reshape(rows, cols, profiles)


def solution(mesh):
    placed = (P("tile", "wave", None), P(), P(), P(None, "tile", "wave"))
    return jax.shard_map(
        shards, mesh=mesh, in_specs=placed, out_specs=P("tile", "wave", None), check_vma=False
    )
```

```python
import jax
import jax.numpy as jnp
from jax import lax
from jax.sharding import PartitionSpec as P


def send(block, axis, step):
    count = lax.axis_size(axis)
    pairs = [(i, i + step) for i in range(count) if 0 <= i + step < count]
    return lax.ppermute(block, axis, pairs)


def window(block, h):
    rows, cols = block.shape[0], block.shape[1]
    top = send(block[rows - h :], "tile", 1)
    bottom = send(block[:h], "tile", -1)
    band = jnp.concatenate([top, block, bottom], axis=0)
    left = send(band[:, cols - h :], "wave", 1)
    right = send(band[:, :h], "wave", -1)
    return jnp.concatenate([left, band, right], axis=1)


def blur_mat(psf, group, cols, h):
    k = psf.shape[0]
    win_cols = cols + 2 * h
    shape_c = (cols, k, win_cols)
    col_gap = lax.broadcasted_iota(jnp.int32, shape_c, 2) - lax.broadcasted_iota(jnp.int32, shape_c, 0)
    hot = (col_gap == lax.broadcasted_iota(jnp.int32, shape_c, 1)).astype(psf.dtype)
    strip = jnp.einsum("ab,xbX->xaX", psf, hot, preferred_element_type=jnp.float32)
    strip = strip.astype(psf.dtype).reshape(cols, k * win_cols)
    total = (group + 2 * h) * win_cols
    blocks = [
        jnp.pad(strip, ((0, 0), (y * win_cols, total - y * win_cols - k * win_cols)))
        for y in range(group)
    ]
    return jnp.concatenate(blocks, axis=0)


def blur(near, mat, group, out_rows, out_cols, h):
    waves = near.shape[-1]
    win_cols = out_cols + 2 * h
    flat = near.reshape(-1, waves)
    span = (group + 2 * h) * win_cols
    outs = [
        jnp.dot(mat, flat[g * win_cols : g * win_cols + span], preferred_element_type=jnp.float32)
        for g in range(0, out_rows, group)
    ]
    return jnp.concatenate(outs, axis=0)


def inside(rows, cols, h):
    top = lax.axis_index("tile") * rows - h
    left = lax.axis_index("wave") * cols - h
    shape = (rows + 2 * h, cols + 2 * h, 1)
    r = lax.broadcasted_iota(jnp.int32, shape, 0) + top
    c = lax.broadcasted_iota(jnp.int32, shape, 1) + left
    total_r = lax.axis_size("tile") * rows
    total_c = lax.axis_size("wave") * cols
    return (r >= 0) & (r < total_r) & (c >= 0) & (c < total_c)


def windows(spectra, measured, h):
    rows, cols, waves = spectra.shape
    wide = 2 * h
    above_s = send(spectra[rows - wide :], "tile", 1)
    below_s = send(spectra[:wide], "tile", -1)
    above_m = send(measured[rows - h :], "tile", 1)
    below_m = send(measured[:h], "tile", -1)
    band_s = jnp.concatenate([above_s, spectra, below_s], axis=0)
    band_m = jnp.concatenate([above_m, measured, below_m], axis=0)
    split = band_s.shape[0] * wide

    def edge(lo_s, lo_m):
        return jnp.concatenate(
            [band_s[:, lo_s : lo_s + wide].reshape(-1, waves), band_m[:, lo_m : lo_m + h].reshape(-1, waves)],
            axis=0,
        )

    left = send(edge(cols - wide, cols - h), "wave", 1)
    right = send(edge(0, 0), "wave", -1)

    def parts(piece):
        return (
            piece[:split].reshape(band_s.shape[0], wide, waves),
            piece[split:].reshape(band_m.shape[0], h, waves),
        )

    left_s, left_m = parts(left)
    right_s, right_m = parts(right)
    near_s = jnp.concatenate([left_s, band_s, right_s], axis=1)
    near_m = jnp.concatenate([left_m, band_m, right_m], axis=1)
    return near_s, near_m


def shards(coefficients, profile_basis, point_spread, observed):
    rows, cols, profiles = coefficients.shape
    waves = profile_basis.shape[1]
    h = point_spread.shape[0] // 2
    opacity = jnp.dot(
        coefficients.reshape(rows * cols, profiles), profile_basis, preferred_element_type=jnp.float32
    )
    spectra = jnp.exp(-opacity).astype(jnp.bfloat16)
    group = 4 if rows % 4 == 0 else rows
    forward = blur_mat(point_spread, group, cols + 2 * h, h)
    adjoint = blur_mat(point_spread[::-1, ::-1], group, cols, h)
    near, measured = windows(spectra.reshape(rows, cols, waves), observed.transpose(1, 2, 0), h)
    blurred = blur(near, forward, group, rows + 2 * h, cols + 2 * h, h)
    blurred = blurred.reshape(rows + 2 * h, cols + 2 * h, waves)
    residual = (blurred - measured.astype(jnp.float32)).astype(jnp.bfloat16)
    residual = jnp.where(inside(rows, cols, h), residual, jnp.zeros_like(residual))
    adjoint_field = blur(residual, adjoint, group, rows, cols, h)
    tau_grad = (-spectra.astype(jnp.float32) * adjoint_field).astype(jnp.bfloat16)
    coef_grad = lax.dot_general(
        tau_grad, profile_basis, (((1,), (1,)), ((), ())), preferred_element_type=jnp.float32
    )
    return coef_grad.astype(jnp.bfloat16).reshape(rows, cols, profiles)


def solution(mesh):
    placed = (P("tile", "wave", None), P(), P(), P(None, "tile", "wave"))
    return jax.shard_map(
        shards, mesh=mesh, in_specs=placed, out_specs=P("tile", "wave", None), check_vma=False
    )
```

```python
import jax
import jax.numpy as jnp
from jax import lax
from jax.sharding import PartitionSpec as P


def send(block, axis, step, pieces=1):
    count = lax.axis_size(axis)
    pairs = [(i, i + step) for i in range(count) if 0 <= i + step < count]
    if pieces == 1 or block.shape[0] % pieces:
        return lax.ppermute(block, axis, pairs)
    size = block.shape[0] // pieces
    parts = [lax.ppermute(block[i * size : (i + 1) * size], axis, pairs) for i in range(pieces)]
    return jnp.concatenate(parts, axis=0)


def window(block, h, pieces=1):
    rows, cols = block.shape[0], block.shape[1]
    top = send(block[rows - h :], "tile", 1, pieces)
    bottom = send(block[:h], "tile", -1, pieces)
    band = jnp.concatenate([top, block, bottom], axis=0)
    left = send(band[:, cols - h :], "wave", 1, pieces)
    right = send(band[:, :h], "wave", -1, pieces)
    return jnp.concatenate([left, band, right], axis=1)


def blur_mat(psf, group, cols, h):
    k = psf.shape[0]
    win_cols = cols + 2 * h
    shape_c = (cols, k, win_cols)
    col_gap = lax.broadcasted_iota(jnp.int32, shape_c, 2) - lax.broadcasted_iota(jnp.int32, shape_c, 0)
    hot = (col_gap == lax.broadcasted_iota(jnp.int32, shape_c, 1)).astype(psf.dtype)
    strip = jnp.einsum("ab,xbX->xaX", psf, hot, preferred_element_type=jnp.float32)
    strip = strip.astype(psf.dtype).reshape(cols, k * win_cols)
    total = (group + 2 * h) * win_cols
    blocks = [
        jnp.pad(strip, ((0, 0), (y * win_cols, total - y * win_cols - k * win_cols)))
        for y in range(group)
    ]
    return jnp.concatenate(blocks, axis=0)


def blur(near, mat, group, out_rows, out_cols, h):
    waves = near.shape[-1]
    win_cols = out_cols + 2 * h
    flat = near.reshape(-1, waves)
    span = (group + 2 * h) * win_cols
    outs = [
        jnp.dot(mat, flat[g * win_cols : g * win_cols + span], preferred_element_type=jnp.float32)
        for g in range(0, out_rows, group)
    ]
    return jnp.concatenate(outs, axis=0)


def inside(rows, cols, h):
    top = lax.axis_index("tile") * rows - h
    left = lax.axis_index("wave") * cols - h
    shape = (rows + 2 * h, cols + 2 * h, 1)
    r = lax.broadcasted_iota(jnp.int32, shape, 0) + top
    c = lax.broadcasted_iota(jnp.int32, shape, 1) + left
    total_r = lax.axis_size("tile") * rows
    total_c = lax.axis_size("wave") * cols
    return (r >= 0) & (r < total_r) & (c >= 0) & (c < total_c)


def shards(coefficients, profile_basis, point_spread, observed):
    rows, cols, profiles = coefficients.shape
    waves = profile_basis.shape[1]
    h = point_spread.shape[0] // 2
    measured = window(observed.transpose(1, 2, 0), h)
    opacity = jnp.dot(
        coefficients.reshape(rows * cols, profiles), profile_basis, preferred_element_type=jnp.float32
    )
    spectra = jnp.exp(-opacity).astype(jnp.bfloat16)
    group = 4 if rows % 4 == 0 else rows
    forward = blur_mat(point_spread, group, cols + 2 * h, h)
    adjoint = blur_mat(point_spread[::-1, ::-1], group, cols, h)
    near = window(spectra.reshape(rows, cols, waves), 2 * h, 2)
    blurred = blur(near, forward, group, rows + 2 * h, cols + 2 * h, h)
    blurred = blurred.reshape(rows + 2 * h, cols + 2 * h, waves)
    residual = (blurred - measured.astype(jnp.float32)).astype(jnp.bfloat16)
    residual = jnp.where(inside(rows, cols, h), residual, jnp.zeros_like(residual))
    adjoint_field = blur(residual, adjoint, group, rows, cols, h)
    tau_grad = (-spectra.astype(jnp.float32) * adjoint_field).astype(jnp.bfloat16)
    coef_grad = lax.dot_general(
        tau_grad, profile_basis, (((1,), (1,)), ((), ())), preferred_element_type=jnp.float32
    )
    return coef_grad.astype(jnp.bfloat16).reshape(rows, cols, profiles)


def solution(mesh):
    placed = (P("tile", "wave", None), P(), P(), P(None, "tile", "wave"))
    return jax.shard_map(
        shards, mesh=mesh, in_specs=placed, out_specs=P("tile", "wave", None), check_vma=False
    )
```

```python
import jax
import numpy as np
import jax.numpy as jnp
from jax import lax
from jax.sharding import PartitionSpec as P


def send(block, axis, step):
    count = lax.axis_size(axis)
    pairs = [(i, i + step) for i in range(count) if 0 <= i + step < count]
    return lax.ppermute(block, axis, pairs)


def pieces(block, h):
    rows, cols = block.shape[0], block.shape[1]
    top = send(block[rows - h :], "tile", 1)
    bottom = send(block[:h], "tile", -1)
    band = jnp.concatenate([top, block, bottom], axis=0)
    left = send(band[:, cols - h :], "wave", 1)
    right = send(band[:, :h], "wave", -1)
    return band, left, right


def window(block, h):
    band, left, right = pieces(block, h)
    return jnp.concatenate([left, band, right], axis=1)


def blur_mat(psf, group, out_cols, h, columns=None):
    k = psf.shape[0]
    if columns is None:
        columns = np.arange(out_cols + 2 * h)
    width = len(columns)
    shape_c = (out_cols, k, width)
    spots = jnp.asarray(np.asarray(columns, np.int32))[None, None, :]
    col_gap = spots - lax.broadcasted_iota(jnp.int32, shape_c, 0)
    hot = (col_gap == lax.broadcasted_iota(jnp.int32, shape_c, 1)).astype(psf.dtype)
    strip = jnp.einsum("ab,xbX->xaX", psf, hot, preferred_element_type=jnp.float32)
    strip = strip.astype(psf.dtype).reshape(out_cols, k * width)
    total = (group + 2 * h) * width
    blocks = [
        jnp.pad(strip, ((0, 0), (y * width, total - y * width - k * width)))
        for y in range(group)
    ]
    return jnp.concatenate(blocks, axis=0)


def blur(near, mat, group, out_rows, h):
    waves = near.shape[-1]
    width = near.shape[1]
    flat = near.reshape(-1, waves)
    span = (group + 2 * h) * width
    outs = [
        jnp.dot(mat, flat[g * width : g * width + span], preferred_element_type=jnp.float32)
        for g in range(0, out_rows, group)
    ]
    return jnp.concatenate(outs, axis=0)


def inside(rows, cols, h):
    top = lax.axis_index("tile") * rows - h
    left = lax.axis_index("wave") * cols - h
    shape = (rows + 2 * h, cols + 2 * h, 1)
    r = lax.broadcasted_iota(jnp.int32, shape, 0) + top
    c = lax.broadcasted_iota(jnp.int32, shape, 1) + left
    total_r = lax.axis_size("tile") * rows
    total_c = lax.axis_size("wave") * cols
    return (r >= 0) & (r < total_r) & (c >= 0) & (c < total_c)


def shards(coefficients, profile_basis, point_spread, observed):
    rows, cols, profiles = coefficients.shape
    waves = profile_basis.shape[1]
    h = point_spread.shape[0] // 2
    measured = window(observed.transpose(1, 2, 0), h)
    opacity = jnp.dot(
        coefficients.reshape(rows * cols, profiles), profile_basis, preferred_element_type=jnp.float32
    )
    spectra = jnp.exp(-opacity).astype(jnp.bfloat16)
    group = 4 if rows % 4 == 0 else rows
    wide = 2 * h
    mid = np.arange(wide, wide + cols)
    side = np.concatenate([np.arange(wide), np.arange(wide + cols, 2 * wide + cols)])
    forward_mid = blur_mat(point_spread, group, cols + 2 * h, h, mid)
    forward_side = blur_mat(point_spread, group, cols + 2 * h, h, side)
    adjoint = blur_mat(point_spread[::-1, ::-1], group, cols, h)
    band, left, right = pieces(spectra.reshape(rows, cols, waves), wide)
    blurred = blur(band, forward_mid, group, rows + 2 * h, h)
    blurred = blurred + blur(jnp.concatenate([left, right], axis=1), forward_side, group, rows + 2 * h, h)
    blurred = blurred.reshape(rows + 2 * h, cols + 2 * h, waves)
    residual = (blurred - measured.astype(jnp.float32)).astype(jnp.bfloat16)
    residual = jnp.where(inside(rows, cols, h), residual, jnp.zeros_like(residual))
    adjoint_field = blur(residual, adjoint, group, rows, h)
    tau_grad = (-spectra.astype(jnp.float32) * adjoint_field).astype(jnp.bfloat16)
    coef_grad = lax.dot_general(
        tau_grad, profile_basis, (((1,), (1,)), ((), ())), preferred_element_type=jnp.float32
    )
    return coef_grad.astype(jnp.bfloat16).reshape(rows, cols, profiles)


def solution(mesh):
    placed = (P("tile", "wave", None), P(), P(), P(None, "tile", "wave"))
    return jax.shard_map(
        shards, mesh=mesh, in_specs=placed, out_specs=P("tile", "wave", None), check_vma=False
    )
```

```python
import jax
import jax.numpy as jnp
from jax import lax
from jax.sharding import PartitionSpec as P


def send(block, axis, step):
    count = lax.axis_size(axis)
    pairs = [(i, i + step) for i in range(count) if 0 <= i + step < count]
    return lax.ppermute(block, axis, pairs)


def window(block, h):
    rows, cols = block.shape[0], block.shape[1]
    top = send(block[rows - h :], "tile", 1)
    bottom = send(block[:h], "tile", -1)
    band = jnp.concatenate([top, block, bottom], axis=0)
    left = send(band[:, cols - h :], "wave", 1)
    right = send(band[:, :h], "wave", -1)
    return jnp.concatenate([left, band, right], axis=1)


def blur_mat(psf, group, cols, h):
    k = psf.shape[0]
    win_cols = cols + 2 * h
    shape_c = (cols, k, win_cols)
    col_gap = lax.broadcasted_iota(jnp.int32, shape_c, 2) - lax.broadcasted_iota(jnp.int32, shape_c, 0)
    hot = (col_gap == lax.broadcasted_iota(jnp.int32, shape_c, 1)).astype(psf.dtype)
    strip = jnp.einsum("ab,xbX->xaX", psf, hot, preferred_element_type=jnp.float32)
    strip = strip.astype(psf.dtype).reshape(cols, k * win_cols)
    total = (group + 2 * h) * win_cols
    blocks = [
        jnp.pad(strip, ((0, 0), (y * win_cols, total - y * win_cols - k * win_cols)))
        for y in range(group)
    ]
    return jnp.concatenate(blocks, axis=0)


def blur(near, mat, group, out_rows, out_cols, h):
    waves = near.shape[-1]
    win_cols = out_cols + 2 * h
    flat = near.reshape(-1, waves)
    span = (group + 2 * h) * win_cols
    outs = [
        jnp.dot(mat, flat[g * win_cols : g * win_cols + span], preferred_element_type=jnp.float32)
        for g in range(0, out_rows, group)
    ]
    return jnp.concatenate(outs, axis=0)


def inside(rows, cols, h):
    top = lax.axis_index("tile") * rows - h
    left = lax.axis_index("wave") * cols - h
    shape = (rows + 2 * h, cols + 2 * h, 1)
    r = lax.broadcasted_iota(jnp.int32, shape, 0) + top
    c = lax.broadcasted_iota(jnp.int32, shape, 1) + left
    total_r = lax.axis_size("tile") * rows
    total_c = lax.axis_size("wave") * cols
    return (r >= 0) & (r < total_r) & (c >= 0) & (c < total_c)


def shards(coefficients, profile_basis, point_spread, observed):
    rows, cols, profiles = coefficients.shape
    waves = profile_basis.shape[1]
    h = point_spread.shape[0] // 2
    measured = window(observed.transpose(1, 2, 0), h)
    opacity = jnp.dot(
        coefficients.reshape(rows * cols, profiles), profile_basis, preferred_element_type=jnp.float32
    )
    spectra = jnp.exp(-opacity).astype(jnp.bfloat16)
    group = 8 if rows % 8 == 0 else rows
    forward = blur_mat(point_spread, group, cols + 2 * h, h)
    adjoint = blur_mat(point_spread[::-1, ::-1], group, cols, h)
    near = window(spectra.reshape(rows, cols, waves), 2 * h)
    blurred = blur(near, forward, group, rows + 2 * h, cols + 2 * h, h)
    blurred = blurred.reshape(rows + 2 * h, cols + 2 * h, waves)
    residual = (blurred - measured.astype(jnp.float32)).astype(jnp.bfloat16)
    residual = jnp.where(inside(rows, cols, h), residual, jnp.zeros_like(residual))
    adjoint_field = blur(residual, adjoint, group, rows, cols, h)
    tau_grad = (-spectra.astype(jnp.float32) * adjoint_field).astype(jnp.bfloat16)
    coef_grad = lax.dot_general(
        tau_grad, profile_basis, (((1,), (1,)), ((), ())), preferred_element_type=jnp.float32
    )
    return coef_grad.astype(jnp.bfloat16).reshape(rows, cols, profiles)


def solution(mesh):
    placed = (P("tile", "wave", None), P(), P(), P(None, "tile", "wave"))
    return jax.shard_map(
        shards, mesh=mesh, in_specs=placed, out_specs=P("tile", "wave", None), check_vma=False
    )
```

```python
import jax
import jax.numpy as jnp
from jax import lax
from jax.sharding import PartitionSpec as P


def send(block, axis, step):
    count = lax.axis_size(axis)
    pairs = [(i, i + step) for i in range(count) if 0 <= i + step < count]
    return lax.ppermute(block, axis, pairs)


def window(block, h):
    rows, cols = block.shape[0], block.shape[1]
    top = send(block[rows - h :], "tile", 1)
    bottom = send(block[:h], "tile", -1)
    band = jnp.concatenate([top, block, bottom], axis=0)
    left = send(band[:, cols - h :], "wave", 1)
    right = send(band[:, :h], "wave", -1)
    return jnp.concatenate([left, band, right], axis=1)


def blur_mat(psf, group, cols, h):
    k = psf.shape[0]
    win_cols = cols + 2 * h
    shape_c = (cols, k, win_cols)
    col_gap = lax.broadcasted_iota(jnp.int32, shape_c, 2) - lax.broadcasted_iota(jnp.int32, shape_c, 0)
    hot = (col_gap == lax.broadcasted_iota(jnp.int32, shape_c, 1)).astype(psf.dtype)
    strip = jnp.einsum("ab,xbX->xaX", psf, hot, preferred_element_type=jnp.float32)
    strip = strip.astype(psf.dtype).reshape(cols, k * win_cols)
    total = (group + 2 * h) * win_cols
    blocks = [
        jnp.pad(strip, ((0, 0), (y * win_cols, total - y * win_cols - k * win_cols)))
        for y in range(group)
    ]
    return jnp.concatenate(blocks, axis=0)


def blur(near, mat, group, out_rows, out_cols, h):
    waves = near.shape[-1]
    win_cols = out_cols + 2 * h
    flat = near.reshape(-1, waves)
    span = (group + 2 * h) * win_cols
    outs = [
        jnp.dot(mat, flat[g * win_cols : g * win_cols + span], preferred_element_type=jnp.float32)
        for g in range(0, out_rows, group)
    ]
    return jnp.concatenate(outs, axis=0)


def inside(rows, cols, h):
    top = lax.axis_index("tile") * rows - h
    left = lax.axis_index("wave") * cols - h
    shape = (rows + 2 * h, cols + 2 * h, 1)
    r = lax.broadcasted_iota(jnp.int32, shape, 0) + top
    c = lax.broadcasted_iota(jnp.int32, shape, 1) + left
    total_r = lax.axis_size("tile") * rows
    total_c = lax.axis_size("wave") * cols
    return (r >= 0) & (r < total_r) & (c >= 0) & (c < total_c)


def shards(coefficients, profile_basis, point_spread, observed):
    rows, cols, profiles = coefficients.shape
    waves = profile_basis.shape[1]
    h = point_spread.shape[0] // 2
    measured = window(observed.transpose(1, 2, 0), h)
    opacity = jnp.dot(
        coefficients.reshape(rows * cols, profiles), profile_basis, preferred_element_type=jnp.float32
    )
    spectra = jnp.exp(-opacity).astype(jnp.bfloat16)
    group = 4 if rows % 4 == 0 else rows
    forward = blur_mat(point_spread, group, cols + 2 * h, h)
    adjoint = blur_mat(point_spread[::-1, ::-1], group, cols, h)
    wide = 2 * h
    block = spectra.reshape(rows, cols, waves)
    top = send(block[rows - wide :], "tile", 1)
    bottom = send(block[:wide], "tile", -1)
    band = jnp.concatenate([top, block, bottom], axis=0)
    left = send(band[:, cols - wide :], "wave", 1)
    right = send(band[:, :wide], "wave", -1)
    span = group + 2 * h
    blurred = jnp.concatenate(
        [
            jnp.dot(
                forward,
                jnp.concatenate(
                    [left[g : g + span], band[g : g + span], right[g : g + span]], axis=1
                ).reshape(-1, waves),
                preferred_element_type=jnp.float32,
            )
            for g in range(0, rows + 2 * h, group)
        ],
        axis=0,
    )
    blurred = blurred.reshape(rows + 2 * h, cols + 2 * h, waves)
    residual = (blurred - measured.astype(jnp.float32)).astype(jnp.bfloat16)
    residual = jnp.where(inside(rows, cols, h), residual, jnp.zeros_like(residual))
    adjoint_field = blur(residual, adjoint, group, rows, cols, h)
    tau_grad = (-spectra.astype(jnp.float32) * adjoint_field).astype(jnp.bfloat16)
    coef_grad = lax.dot_general(
        tau_grad, profile_basis, (((1,), (1,)), ((), ())), preferred_element_type=jnp.float32
    )
    return coef_grad.astype(jnp.bfloat16).reshape(rows, cols, profiles)


def solution(mesh):
    placed = (P("tile", "wave", None), P(), P(), P(None, "tile", "wave"))
    return jax.shard_map(
        shards, mesh=mesh, in_specs=placed, out_specs=P("tile", "wave", None), check_vma=False
    )
```

```python
import jax
import jax.numpy as jnp
from jax import lax
from jax.sharding import PartitionSpec as P


def send(block, axis, step):
    count = lax.axis_size(axis)
    pairs = [(i, i + step) for i in range(count) if 0 <= i + step < count]
    return lax.ppermute(block, axis, pairs)


def window(block, h, after=None):
    rows, cols = block.shape[0], block.shape[1]
    if after is not None:
        after, block = lax.optimization_barrier((after, block))
    top = send(block[rows - h :], "tile", 1)
    bottom = send(block[:h], "tile", -1)
    band = jnp.concatenate([top, block, bottom], axis=0)
    left = send(band[:, cols - h :], "wave", 1)
    right = send(band[:, :h], "wave", -1)
    return jnp.concatenate([left, band, right], axis=1)


def blur_mat(psf, group, cols, h):
    k = psf.shape[0]
    win_cols = cols + 2 * h
    shape_c = (cols, k, win_cols)
    col_gap = lax.broadcasted_iota(jnp.int32, shape_c, 2) - lax.broadcasted_iota(jnp.int32, shape_c, 0)
    hot = (col_gap == lax.broadcasted_iota(jnp.int32, shape_c, 1)).astype(psf.dtype)
    strip = jnp.einsum("ab,xbX->xaX", psf, hot, preferred_element_type=jnp.float32)
    strip = strip.astype(psf.dtype).reshape(cols, k * win_cols)
    total = (group + 2 * h) * win_cols
    blocks = [
        jnp.pad(strip, ((0, 0), (y * win_cols, total - y * win_cols - k * win_cols)))
        for y in range(group)
    ]
    return jnp.concatenate(blocks, axis=0)


def blur(near, mat, group, out_rows, out_cols, h):
    waves = near.shape[-1]
    win_cols = out_cols + 2 * h
    flat = near.reshape(-1, waves)
    span = (group + 2 * h) * win_cols
    outs = [
        jnp.dot(mat, flat[g * win_cols : g * win_cols + span], preferred_element_type=jnp.float32)
        for g in range(0, out_rows, group)
    ]
    return jnp.concatenate(outs, axis=0)


def inside(rows, cols, h):
    top = lax.axis_index("tile") * rows - h
    left = lax.axis_index("wave") * cols - h
    shape = (rows + 2 * h, cols + 2 * h, 1)
    r = lax.broadcasted_iota(jnp.int32, shape, 0) + top
    c = lax.broadcasted_iota(jnp.int32, shape, 1) + left
    total_r = lax.axis_size("tile") * rows
    total_c = lax.axis_size("wave") * cols
    return (r >= 0) & (r < total_r) & (c >= 0) & (c < total_c)


def shards(coefficients, profile_basis, point_spread, observed):
    rows, cols, profiles = coefficients.shape
    waves = profile_basis.shape[1]
    h = point_spread.shape[0] // 2
    opacity = jnp.dot(
        coefficients.reshape(rows * cols, profiles), profile_basis, preferred_element_type=jnp.float32
    )
    spectra = jnp.exp(-opacity).astype(jnp.bfloat16)
    group = 4 if rows % 4 == 0 else rows
    forward = blur_mat(point_spread, group, cols + 2 * h, h)
    adjoint = blur_mat(point_spread[::-1, ::-1], group, cols, h)
    block = spectra.reshape(rows, cols, waves)
    wide = 2 * h
    top = send(block[rows - wide :], "tile", 1)
    bottom = send(block[:wide], "tile", -1)
    measured = window(observed.transpose(1, 2, 0), h, (top, bottom))
    band = jnp.concatenate([top, block, bottom], axis=0)
    left = send(band[:, cols - wide :], "wave", 1)
    right = send(band[:, :wide], "wave", -1)
    near = jnp.concatenate([left, band, right], axis=1)
    blurred = blur(near, forward, group, rows + 2 * h, cols + 2 * h, h)
    blurred = blurred.reshape(rows + 2 * h, cols + 2 * h, waves)
    residual = (blurred - measured.astype(jnp.float32)).astype(jnp.bfloat16)
    residual = jnp.where(inside(rows, cols, h), residual, jnp.zeros_like(residual))
    adjoint_field = blur(residual, adjoint, group, rows, cols, h)
    tau_grad = (-spectra.astype(jnp.float32) * adjoint_field).astype(jnp.bfloat16)
    coef_grad = lax.dot_general(
        tau_grad, profile_basis, (((1,), (1,)), ((), ())), preferred_element_type=jnp.float32
    )
    return coef_grad.astype(jnp.bfloat16).reshape(rows, cols, profiles)


def solution(mesh):
    placed = (P("tile", "wave", None), P(), P(), P(None, "tile", "wave"))
    return jax.shard_map(
        shards, mesh=mesh, in_specs=placed, out_specs=P("tile", "wave", None), check_vma=False
    )
```

```python
import jax
import jax.numpy as jnp
from jax import lax
from jax.sharding import PartitionSpec as P


def send(block, axis, step):
    count = lax.axis_size(axis)
    pairs = [(i, i + step) for i in range(count) if 0 <= i + step < count]
    return lax.ppermute(block, axis, pairs)


def window(block, h):
    rows, cols = block.shape[0], block.shape[1]
    top = send(block[rows - h :], "tile", 1)
    bottom = send(block[:h], "tile", -1)
    band = jnp.concatenate([top, block, bottom], axis=0)
    left = send(band[:, cols - h :], "wave", 1)
    right = send(band[:, :h], "wave", -1)
    return jnp.concatenate([left, band, right], axis=1)


def blur_mat(psf, group, cols, h):
    k = psf.shape[0]
    win_cols = cols + 2 * h
    shape_c = (cols, k, win_cols)
    col_gap = lax.broadcasted_iota(jnp.int32, shape_c, 2) - lax.broadcasted_iota(jnp.int32, shape_c, 0)
    hot = (col_gap == lax.broadcasted_iota(jnp.int32, shape_c, 1)).astype(psf.dtype)
    strip = jnp.einsum("ab,xbX->xaX", psf, hot, preferred_element_type=jnp.float32)
    strip = strip.astype(psf.dtype).reshape(cols, k * win_cols)
    total = (group + 2 * h) * win_cols
    blocks = [
        jnp.pad(strip, ((0, 0), (y * win_cols, total - y * win_cols - k * win_cols)))
        for y in range(group)
    ]
    return jnp.concatenate(blocks, axis=0)


def blur(near, mat, group, out_rows, out_cols, h):
    waves = near.shape[-1]
    win_cols = out_cols + 2 * h
    flat = near.reshape(-1, waves)
    span = (group + 2 * h) * win_cols
    outs = [
        jnp.dot(mat, flat[g * win_cols : g * win_cols + span], preferred_element_type=jnp.float32)
        for g in range(0, out_rows, group)
    ]
    return jnp.concatenate(outs, axis=0)


def inside(rows, cols, h):
    top = lax.axis_index("tile") * rows - h
    left = lax.axis_index("wave") * cols - h
    shape = (rows + 2 * h, cols + 2 * h, 1)
    r = lax.broadcasted_iota(jnp.int32, shape, 0) + top
    c = lax.broadcasted_iota(jnp.int32, shape, 1) + left
    total_r = lax.axis_size("tile") * rows
    total_c = lax.axis_size("wave") * cols
    return (r >= 0) & (r < total_r) & (c >= 0) & (c < total_c)


def shards(coefficients, profile_basis, point_spread, observed):
    rows, cols, profiles = coefficients.shape
    waves = profile_basis.shape[1]
    h = point_spread.shape[0] // 2
    measured = window(observed.transpose(1, 2, 0), h)
    measured, coefficients = lax.optimization_barrier((measured, coefficients))
    opacity = jnp.dot(
        coefficients.reshape(rows * cols, profiles), profile_basis, preferred_element_type=jnp.float32
    )
    spectra = jnp.exp(-opacity).astype(jnp.bfloat16)
    group = 4 if rows % 4 == 0 else rows
    forward = blur_mat(point_spread, group, cols + 2 * h, h)
    adjoint = blur_mat(point_spread[::-1, ::-1], group, cols, h)
    near = window(spectra.reshape(rows, cols, waves), 2 * h)
    blurred = blur(near, forward, group, rows + 2 * h, cols + 2 * h, h)
    blurred = blurred.reshape(rows + 2 * h, cols + 2 * h, waves)
    residual = (blurred - measured.astype(jnp.float32)).astype(jnp.bfloat16)
    residual = jnp.where(inside(rows, cols, h), residual, jnp.zeros_like(residual))
    adjoint_field = blur(residual, adjoint, group, rows, cols, h)
    tau_grad = (-spectra.astype(jnp.float32) * adjoint_field).astype(jnp.bfloat16)
    coef_grad = lax.dot_general(
        tau_grad, profile_basis, (((1,), (1,)), ((), ())), preferred_element_type=jnp.float32
    )
    return coef_grad.astype(jnp.bfloat16).reshape(rows, cols, profiles)


def solution(mesh):
    placed = (P("tile", "wave", None), P(), P(), P(None, "tile", "wave"))
    return jax.shard_map(
        shards, mesh=mesh, in_specs=placed, out_specs=P("tile", "wave", None), check_vma=False
    )
```

```python
import jax
import jax.numpy as jnp
from jax import lax
from jax.sharding import PartitionSpec as P


def send(block, axis, step):
    count = lax.axis_size(axis)
    pairs = [(i, i + step) for i in range(count) if 0 <= i + step < count]
    return lax.ppermute(block, axis, pairs)


def window(block, h):
    rows, cols = block.shape[0], block.shape[1]
    top = send(block[rows - h :], "tile", 1)
    bottom = send(block[:h], "tile", -1)
    band = jnp.concatenate([top, block, bottom], axis=0)
    left = send(band[:, cols - h :], "wave", 1)
    right = send(band[:, :h], "wave", -1)
    return jnp.concatenate([left, band, right], axis=1)


def blur_mat(psf, group, cols, h):
    k = psf.shape[0]
    win_cols = cols + 2 * h
    shape_c = (cols, k, win_cols)
    col_gap = lax.broadcasted_iota(jnp.int32, shape_c, 2) - lax.broadcasted_iota(jnp.int32, shape_c, 0)
    hot = (col_gap == lax.broadcasted_iota(jnp.int32, shape_c, 1)).astype(psf.dtype)
    strip = jnp.einsum("ab,xbX->xaX", psf, hot, preferred_element_type=jnp.float32)
    strip = strip.astype(psf.dtype).reshape(cols, k * win_cols)
    total = (group + 2 * h) * win_cols
    blocks = [
        jnp.pad(strip, ((0, 0), (y * win_cols, total - y * win_cols - k * win_cols)))
        for y in range(group)
    ]
    return jnp.concatenate(blocks, axis=0)


def blur(near, mat, group, out_rows, out_cols, h):
    waves = near.shape[-1]
    win_cols = out_cols + 2 * h
    flat = near.reshape(-1, waves)
    span = (group + 2 * h) * win_cols
    outs = [
        jnp.dot(mat, flat[g * win_cols : g * win_cols + span], preferred_element_type=jnp.float32)
        for g in range(0, out_rows, group)
    ]
    return jnp.concatenate(outs, axis=0)


def inside(rows, cols, h):
    top = lax.axis_index("tile") * rows - h
    left = lax.axis_index("wave") * cols - h
    shape = (rows + 2 * h, cols + 2 * h, 1)
    r = lax.broadcasted_iota(jnp.int32, shape, 0) + top
    c = lax.broadcasted_iota(jnp.int32, shape, 1) + left
    total_r = lax.axis_size("tile") * rows
    total_c = lax.axis_size("wave") * cols
    return (r >= 0) & (r < total_r) & (c >= 0) & (c < total_c)


def shards(coefficients, profile_basis, point_spread, observed):
    rows, cols, profiles = coefficients.shape
    waves = profile_basis.shape[1]
    h = point_spread.shape[0] // 2
    measured = window(observed.transpose(1, 2, 0), h)
    opacity = jnp.dot(
        coefficients.reshape(rows * cols, profiles), profile_basis, preferred_element_type=jnp.float32
    )
    spectra = jnp.exp(-opacity).astype(jnp.bfloat16)
    group = 4 if rows % 4 == 0 else rows
    forward = blur_mat(point_spread, group, cols + 2 * h, h)
    adjoint = blur_mat(point_spread[::-1, ::-1], group, cols, h)
    block = spectra.reshape(rows, cols, waves)
    wide = 2 * h
    top = send(block[rows - wide :], "tile", 1)
    bottom = send(block[:wide], "tile", -1)
    band = jnp.concatenate([top, block, bottom], axis=0)
    measured, band = lax.optimization_barrier((measured, band))
    left = send(band[:, cols - wide :], "wave", 1)
    right = send(band[:, :wide], "wave", -1)
    near = jnp.concatenate([left, band, right], axis=1)
    blurred = blur(near, forward, group, rows + 2 * h, cols + 2 * h, h)
    blurred = blurred.reshape(rows + 2 * h, cols + 2 * h, waves)
    residual = (blurred - measured.astype(jnp.float32)).astype(jnp.bfloat16)
    residual = jnp.where(inside(rows, cols, h), residual, jnp.zeros_like(residual))
    adjoint_field = blur(residual, adjoint, group, rows, cols, h)
    tau_grad = (-spectra.astype(jnp.float32) * adjoint_field).astype(jnp.bfloat16)
    coef_grad = lax.dot_general(
        tau_grad, profile_basis, (((1,), (1,)), ((), ())), preferred_element_type=jnp.float32
    )
    return coef_grad.astype(jnp.bfloat16).reshape(rows, cols, profiles)


def solution(mesh):
    placed = (P("tile", "wave", None), P(), P(), P(None, "tile", "wave"))
    return jax.shard_map(
        shards, mesh=mesh, in_specs=placed, out_specs=P("tile", "wave", None), check_vma=False
    )
```

```python
import jax
import jax.numpy as jnp
from jax import lax
from jax.sharding import PartitionSpec as P


def send(block, axis, step):
    count = lax.axis_size(axis)
    pairs = [(i, i + step) for i in range(count) if 0 <= i + step < count]
    return lax.ppermute(block, axis, pairs)


def window(block, h):
    rows, cols = block.shape[0], block.shape[1]
    top = send(block[rows - h :], "tile", 1)
    bottom = send(block[:h], "tile", -1)
    band = jnp.concatenate([top, block, bottom], axis=0)
    left = send(band[:, cols - h :], "wave", 1)
    right = send(band[:, :h], "wave", -1)
    return jnp.concatenate([left, band, right], axis=1)


def blur_mat(psf, group, cols, h):
    k = psf.shape[0]
    win_cols = cols + 2 * h
    shape_c = (cols, k, win_cols)
    col_gap = lax.broadcasted_iota(jnp.int32, shape_c, 2) - lax.broadcasted_iota(jnp.int32, shape_c, 0)
    hot = (col_gap == lax.broadcasted_iota(jnp.int32, shape_c, 1)).astype(psf.dtype)
    strip = jnp.einsum("ab,xbX->xaX", psf, hot, preferred_element_type=jnp.float32)
    strip = strip.astype(psf.dtype).reshape(cols, k * win_cols)
    total = (group + 2 * h) * win_cols
    blocks = [
        jnp.pad(strip, ((0, 0), (y * win_cols, total - y * win_cols - k * win_cols)))
        for y in range(group)
    ]
    return jnp.concatenate(blocks, axis=0)


def blur(near, mat, group, out_rows, out_cols, h):
    waves = near.shape[-1]
    win_cols = out_cols + 2 * h
    flat = near.reshape(-1, waves)
    span = (group + 2 * h) * win_cols
    outs = [
        jnp.dot(mat, flat[g * win_cols : g * win_cols + span], preferred_element_type=jnp.float32)
        for g in range(0, out_rows, group)
    ]
    return jnp.concatenate(outs, axis=0)


def inside(rows, cols, h):
    top = lax.axis_index("tile") * rows - h
    left = lax.axis_index("wave") * cols - h
    shape = (rows + 2 * h, cols + 2 * h, 1)
    r = lax.broadcasted_iota(jnp.int32, shape, 0) + top
    c = lax.broadcasted_iota(jnp.int32, shape, 1) + left
    total_r = lax.axis_size("tile") * rows
    total_c = lax.axis_size("wave") * cols
    return (r >= 0) & (r < total_r) & (c >= 0) & (c < total_c)


def shards(coefficients, profile_basis, point_spread, observed):
    rows, cols, profiles = coefficients.shape
    waves = profile_basis.shape[1]
    h = point_spread.shape[0] // 2
    measured = window(observed.transpose(1, 2, 0), h)
    opacity = jnp.dot(
        coefficients.reshape(rows * cols, profiles), profile_basis, preferred_element_type=jnp.float32
    )
    spectra = jnp.exp(-opacity).astype(jnp.bfloat16)
    group = 4 if rows % 4 == 0 else rows
    forward = blur_mat(point_spread, group, cols + 2 * h, h)
    adjoint = blur_mat(point_spread[::-1, ::-1], rows, cols, h)
    near = window(spectra.reshape(rows, cols, waves), 2 * h)
    blurred = blur(near, forward, group, rows + 2 * h, cols + 2 * h, h)
    blurred = blurred.reshape(rows + 2 * h, cols + 2 * h, waves)
    residual = (blurred - measured.astype(jnp.float32)).astype(jnp.bfloat16)
    residual = jnp.where(inside(rows, cols, h), residual, jnp.zeros_like(residual))
    adjoint_field = blur(residual, adjoint, rows, rows, cols, h)
    tau_grad = (-spectra.astype(jnp.float32) * adjoint_field).astype(jnp.bfloat16)
    coef_grad = lax.dot_general(
        tau_grad, profile_basis, (((1,), (1,)), ((), ())), preferred_element_type=jnp.float32
    )
    return coef_grad.astype(jnp.bfloat16).reshape(rows, cols, profiles)


def solution(mesh):
    placed = (P("tile", "wave", None), P(), P(), P(None, "tile", "wave"))
    return jax.shard_map(
        shards, mesh=mesh, in_specs=placed, out_specs=P("tile", "wave", None), check_vma=False
    )
```
